256 devices in a mesh: chan: 8 (over z_hi, x), tm: 16 (over z_lo, y), dp: 2 (over core).
Axes of the slice: x: 4, y: 4, z: 8 (z_hi: 2, z_lo: 4; z = z_hi * 4 + z_lo), core: 2. Of those that a mesh axis runs over, the one named last changes fastest.
Arguments:
- contexts: bfloat16 [512, 4, 16384], P('tm', 'dp', 'chan'), may hold values from -6 to 6
- cotangent: bfloat16 [512, 4, 16384], P('tm', 'dp', 'chan'), may hold values from -6 to 6
- w_in: bfloat16 [16384, 8192], P('chan', 'tm'), may hold values from -0.046875 to 0.046875
- w_out: bfloat16 [8192, 16384], P('tm', 'chan'), may hold values from -0.0625 to 0.0625
- time_weight: bfloat16 [512, 512], replicated, may hold values from -0.25 to 0.25
Outputs:
- grad_contexts: bfloat16 [512, 4, 16384], P('tm', 'dp', 'chan')
- grad_w_in: float32 [16384, 8192], P('chan', ('tm', 'dp'))
- grad_w_out: float32 [8192, 16384], P(('tm', 'dp'), 'chan')
- grad_time: float32 [512, 512], replicated
The draws below stay inside these ranges and needn't reach their ends.
All inputs are finite; a program needn't handle non-finite values.
Results may differ from the reference program's by a relative error of at most 0.0057.
Values may be sent and summed in bfloat16 or wider, within the bound.
No kernel may reach another device: no remote copies, remote signals or barrier semaphores. Data moves between devices by JAX's collectives and lax.ppermute only.
A program may use at most 192 MiB of HBM per device.

```python
import math
import jax
import jax.numpy as jnp

CHANNELS = 16384
HIDDEN_SIZE = 8192
LEN = 512
WIN = 4


def block_levels(rng, extent, cuts, least, top_value):
    def one(axis_at, blocks):
        draws = jax.random.uniform(jax.random.fold_in(jax.random.fold_in(rng, 6), axis_at), (blocks,), jnp.float32, least / len(cuts), top_value / len(cuts))
        return jnp.repeat(jnp.exp(draws), extent[axis_at] // blocks).reshape((-1,) + (1,) * (len(extent) - axis_at - 1))

    loudness = one(*cuts[0])
    for cut in cuts[1:]:
        loudness = loudness * one(*cut)
    return loudness


def gaussian(key, extent, scale, bound, pieces=(), held_as=jnp.bfloat16):
    gain = block_levels(key, extent, pieces, -0.22, 0.18) if pieces else 1.0
    array = jax.random.normal(key, extent, jnp.float32) * scale * gain
    return jnp.minimum(jnp.maximum(array, -bound), bound).astype(held_as)


def setup_inputs(seed: int = 0) -> dict:
    splits = jax.random.split(jax.random.key(seed), 6)
    contexts = gaussian(splits[0], (LEN, WIN, CHANNELS), 1.0, 6.0, ((0, 16), (1, 2), (2, 8)))
    cotangent = gaussian(splits[1], (LEN, WIN, CHANNELS), 1.0, 6.0, ((0, 16), (1, 2), (2, 8)))
    w_in = gaussian(splits[2], (CHANNELS, HIDDEN_SIZE), CHANNELS ** -0.5, 0.046875, ((0, 8), (1, 16)))
    w_out = gaussian(splits[3], (HIDDEN_SIZE, CHANNELS), HIDDEN_SIZE ** -0.5, 0.0625, ((0, 16), (1, 8)))
    time_weight = gaussian(splits[4], (LEN, LEN), LEN ** -0.5, 0.25)
    return dict(contexts=contexts, cotangent=cotangent, w_in=w_in, w_out=w_out, time_weight=time_weight)


tanh_scale = math.sqrt(2.0 / math.pi)
cubic_term = 0.044715

def gelu_pair(value):
    inner = jnp.tanh(tanh_scale * (value + cubic_term * value * value * value))
    result = 0.5 * value * (1.0 + inner)
    slope = 0.5 * (1.0 + inner) + 0.5 * value * (1.0 - inner * inner) * tanh_scale * (1.0 + 3.0 * cubic_term * value * value)
    return (result, slope)

def reference(contexts, cotangent, w_in, w_out, time_weight):
    length, windows, channels = contexts.shape
    flat_x = contexts.reshape(length, windows * channels)
    pre_time = jnp.dot(time_weight, flat_x, preferred_element_type=jnp.float32)
    act_time, slope_time = gelu_pair(pre_time)
    mixed = (flat_x.astype(jnp.float32) + act_time).astype(jnp.bfloat16).reshape(length * windows, channels)
    grad_rows = cotangent.reshape(length * windows, channels)
    hidden_pre = jnp.dot(mixed, w_in, preferred_element_type=jnp.float32)
    hidden_grad = jnp.dot(grad_rows, w_out.T, preferred_element_type=jnp.float32)
    act_hidden, slope_hidden = gelu_pair(hidden_pre)
    activation = act_hidden.astype(jnp.bfloat16)
    pre_grad = (hidden_grad * slope_hidden).astype(jnp.bfloat16)
    grad_w_in = jnp.dot(mixed.T, pre_grad, preferred_element_type=jnp.float32)
    grad_w_out = jnp.dot(activation.T, grad_rows, preferred_element_type=jnp.float32)
    mixed_grad = grad_rows.astype(jnp.float32) + jnp.dot(pre_grad, w_in.T, preferred_element_type=jnp.float32)
    time_gate = (mixed_grad.reshape(length, windows * channels) * slope_time).astype(jnp.bfloat16)
    back = jnp.dot(time_weight.T, time_gate, preferred_element_type=jnp.float32)
    grad_contexts = (mixed_grad.reshape(length, windows * channels) + back).astype(jnp.bfloat16).reshape(length, windows, channels)
    grad_time = jnp.dot(time_gate, flat_x.T, preferred_element_type=jnp.float32)
    return (grad_contexts, grad_w_in, grad_w_out, grad_time)
```

```python
import math

import jax
import jax.numpy as jnp
from jax import lax
from jax.sharding import PartitionSpec as P

tanh_scale = math.sqrt(2.0 / math.pi)
cubic_term = 0.044715


def gelu_pair(value):
    inner = jnp.tanh(tanh_scale * (value + cubic_term * value * value * value))
    result = 0.5 * value * (1.0 + inner)
    slope = 0.5 * (1.0 + inner) + 0.5 * value * (1.0 - inner * inner) * tanh_scale * (
        1.0 + 3.0 * cubic_term * value * value
    )
    return (result, slope)


def hidden_finish(hidden_pre, hidden_grad):
    act_hidden, slope_hidden = gelu_pair(hidden_pre)
    return (act_hidden.astype(jnp.bfloat16), (hidden_grad * slope_hidden).astype(jnp.bfloat16))


def gather_a2a(x, axis_name, size, axis):
    b = jnp.broadcast_to(x[None], (size,) + x.shape)
    y = lax.all_to_all(b, axis_name, 0, 0, tiled=True)
    y = jnp.moveaxis(y, 0, axis)
    shape = list(x.shape)
    shape[axis] *= size
    return y.reshape(shape)


def scatter_a2a(p, axis_name, size):
    y = lax.all_to_all(p.reshape((size, p.shape[0] // size) + p.shape[1:]), axis_name, 0, 0, tiled=True)
    return y.sum(0)


def on_device(contexts, cotangent, w_in, w_out, time_weight, tm, chan, everyone, world):
    local_len, batch_dev, width_dev = contexts.shape
    pair = lax.all_gather(jnp.stack([contexts, cotangent]), "tm", axis=1, tiled=True)
    whole_x, whole_dy = pair[0], pair[1]
    length = whole_x.shape[0]
    flat_x = whole_x.reshape(length, batch_dev * width_dev)
    pre_time = jnp.dot(time_weight, flat_x, preferred_element_type=jnp.float32)
    act_time, slope_time = gelu_pair(pre_time)
    mixed = (
        (flat_x.astype(jnp.float32) + act_time)
        .astype(jnp.bfloat16)
        .reshape(length * batch_dev, width_dev)
    )
    grad_rows = whole_dy.reshape(length * batch_dev, width_dev)
    hidden_part = jnp.dot(mixed, w_in, preferred_element_type=jnp.float32)
    hgrad_part = jnp.einsum("rc,hc->rh", grad_rows, w_out, preferred_element_type=jnp.float32)
    hidden_pre, hidden_grad = scatter_a2a(jnp.stack([hidden_part, hgrad_part], 1), "chan", chan).swapaxes(0, 1)
    act_rows, grad_rows_h = hidden_finish(hidden_pre, hidden_grad)
    fin = gather_a2a(jnp.stack([act_rows, grad_rows_h], 1), "chan", chan, 0)
    activation, pre_grad = fin[:, 0], fin[:, 1]
    win_part = jnp.einsum("rc,rh->ch", mixed, pre_grad, preferred_element_type=jnp.float32)
    wout_part = jnp.einsum("rh,rc->hc", activation, grad_rows, preferred_element_type=jnp.float32)
    grad_w_in, grad_w_out = (
        lax.psum_scatter(win_part, "dp", scatter_dimension=1, tiled=True),
        lax.psum_scatter(wout_part, "dp", scatter_dimension=0, tiled=True),
    )
    share = jnp.einsum("rh,ch->rc", pre_grad, w_in, preferred_element_type=jnp.float32) + grad_rows.astype(
        jnp.float32
    ) * (1.0 / tm)
    share = share.reshape(length, batch_dev * width_dev)
    gate = share * slope_time
    gate_hi = gate.astype(jnp.bfloat16)
    gate_lo = (gate - gate_hi.astype(jnp.float32)).astype(jnp.bfloat16)
    gate = jnp.concatenate([gate_hi, gate_lo], axis=0)
    twice = jnp.concatenate([time_weight, time_weight], axis=0)
    back = jnp.einsum("tl,tk->lk", twice, gate, preferred_element_type=jnp.float32)
    grad_contexts = (
        lax.psum_scatter(share + back, "tm", scatter_dimension=0, tiled=True)
        .reshape(local_len, batch_dev, width_dev)
        .astype(jnp.bfloat16)
    )
    time_part = jnp.einsum("tk,lk->tl", gate_hi, flat_x, preferred_element_type=jnp.float32) + jnp.einsum(
        "tk,lk->tl", gate_lo, flat_x, preferred_element_type=jnp.float32
    )
    grad_time = gather_a2a(scatter_a2a(time_part, everyone, world), everyone, world, 0)
    return (grad_contexts, grad_w_in, grad_w_out, grad_time)


def solution(mesh):
    import functools

    step = functools.partial(
        on_device,
        tm=mesh.shape["tm"],
        chan=mesh.shape["chan"],
        everyone=("chan", "tm", "dp"),
        world=mesh.size,
    )
    return jax.shard_map(
        step,
        mesh=mesh,
        in_specs=(
            P("tm", "dp", "chan"),
            P("tm", "dp", "chan"),
            P("chan", "tm"),
            P("tm", "chan"),
            P(),
        ),
        out_specs=(P("tm", "dp", "chan"), P("chan", ("tm", "dp")), P(("tm", "dp"), "chan"), P()),
        check_vma=False,
    )
```

```python
import functools
import math

import jax
import jax.numpy as jnp
from jax import lax
from jax.sharding import PartitionSpec as P

tanh_scale = math.sqrt(2.0 / math.pi)
cubic_term = 0.044715


def gelu_pair(value):
    inner = jnp.tanh(tanh_scale * (value + cubic_term * value * value * value))
    result = 0.5 * value * (1.0 + inner)
    slope = 0.5 * (1.0 + inner) + 0.5 * value * (1.0 - inner * inner) * tanh_scale * (
        1.0 + 3.0 * cubic_term * value * value
    )
    return (result, slope)


def hidden_finish(hidden_pre, hidden_grad):
    act_hidden, slope_hidden = gelu_pair(hidden_pre)
    return (act_hidden.astype(jnp.bfloat16), (hidden_grad * slope_hidden).astype(jnp.bfloat16))


def gather_a2a(x, axis_name, size):
    b = jnp.broadcast_to(x[None], (size,) + x.shape)
    y = lax.all_to_all(b, axis_name, 0, 0, tiled=True)
    return y.reshape((size * x.shape[0],) + x.shape[1:])


def scatter_a2a(p, axis_name, size):
    y = lax.all_to_all(p.reshape((size, p.shape[0] // size) + p.shape[1:]), axis_name, 0, 0, tiled=True)
    return y.sum(0)


def on_device(contexts, cotangent, w_in, w_out, time_weight, tm, chan, everyone, world):
    local_len, batch_dev, width_dev = contexts.shape
    own = jnp.stack([contexts, cotangent]).transpose(0, 2, 1, 3)
    pair = lax.all_gather(own, "tm", axis=2, tiled=True)
    whole_x, whole_dy = pair[0], pair[1]
    length = whole_x.shape[1]
    pre_time = jnp.einsum("tl,blc->btc", time_weight, whole_x, preferred_element_type=jnp.float32)
    act_time, slope_time = gelu_pair(pre_time)
    mixed = (whole_x.astype(jnp.float32) + act_time).astype(jnp.bfloat16)
    rows = batch_dev * length
    mixed_rows = mixed.reshape(rows, width_dev)
    grad_rows = whole_dy.reshape(rows, width_dev)
    hidden_part = jnp.dot(mixed_rows, w_in, preferred_element_type=jnp.float32)
    hgrad_part = jnp.einsum("rc,hc->rh", grad_rows, w_out, preferred_element_type=jnp.float32)
    summed = scatter_a2a(jnp.stack([hidden_part, hgrad_part], 1), "chan", chan)
    act_rows, pre_grad_rows = hidden_finish(summed[:, 0], summed[:, 1])
    fin = gather_a2a(jnp.stack([act_rows, pre_grad_rows], 1), "chan", chan)
    activation, pre_grad = fin[:, 0], fin[:, 1]
    win_part = jnp.einsum("rc,rh->ch", mixed_rows, pre_grad, preferred_element_type=jnp.float32)
    wout_part = jnp.einsum("rh,rc->hc", activation, grad_rows, preferred_element_type=jnp.float32)
    grad_w_in, grad_w_out = (
        lax.psum_scatter(win_part, "dp", scatter_dimension=1, tiled=True),
        lax.psum_scatter(wout_part, "dp", scatter_dimension=0, tiled=True),
    )
    share = jnp.einsum("rh,ch->rc", pre_grad, w_in, preferred_element_type=jnp.float32) + grad_rows.astype(
        jnp.float32
    ) * (1.0 / tm)
    share = share.reshape(batch_dev, length, width_dev)
    gate = (share * slope_time).astype(jnp.bfloat16)
    back = jnp.einsum("tl,btc->blc", time_weight, gate, preferred_element_type=jnp.float32)
    grad_own = lax.psum_scatter(share + back, "tm", scatter_dimension=1, tiled=True)
    grad_contexts = grad_own.astype(jnp.bfloat16).transpose(1, 0, 2)
    time_part = jnp.einsum("btc,blc->tl", gate, whole_x, preferred_element_type=jnp.float32)
    grad_time = gather_a2a(scatter_a2a(time_part, everyone, world), everyone, world)
    return (grad_contexts, grad_w_in, grad_w_out, grad_time)


def solution(mesh):
    step = functools.partial(
        on_device,
        tm=mesh.shape["tm"],
        chan=mesh.shape["chan"],
        everyone=("chan", "tm", "dp"),
        world=mesh.size,
    )
    return jax.shard_map(
        step,
        mesh=mesh,
        in_specs=(
            P("tm", "dp", "chan"),
            P("tm", "dp", "chan"),
            P("chan", "tm"),
            P("tm", "chan"),
            P(),
        ),
        out_specs=(P("tm", "dp", "chan"), P("chan", ("tm", "dp")), P(("tm", "dp"), "chan"), P()),
        check_vma=False,
    )
```

```python
import functools
import math

import jax
import jax.numpy as jnp
from jax import lax
from jax.sharding import Mesh
from jax.sharding import PartitionSpec as P

TM = ("tz", "ty")
CHAN = ("zh", "cx")
tanh_scale = math.sqrt(2.0 / math.pi)
cubic_term = 0.044715


def gelu_pair(value):
    inner = jnp.tanh(tanh_scale * (value + cubic_term * value * value * value))
    result = 0.5 * value * (1.0 + inner)
    slope = 0.5 * (1.0 + inner) + 0.5 * value * (1.0 - inner * inner) * tanh_scale * (
        1.0 + 3.0 * cubic_term * value * value
    )
    return (result, slope)


def hidden_finish(hidden_pre, hidden_grad):
    act_hidden, slope_hidden = gelu_pair(hidden_pre)
    return (act_hidden.astype(jnp.bfloat16), (hidden_grad * slope_hidden).astype(jnp.bfloat16))


def gather_a2a(x, axis_name, size):
    b = jnp.broadcast_to(x[None], (size,) + x.shape)
    y = lax.all_to_all(b, axis_name, 0, 0, tiled=True)
    return y.reshape((size * x.shape[0],) + x.shape[1:])


def scatter_a2a(p, axis_name, size):
    y = lax.all_to_all(p.reshape((size, p.shape[0] // size) + p.shape[1:]), axis_name, 0, 0, tiled=True)
    return y.sum(0)


def on_device(contexts, cotangent, w_in, w_out, time_weight, tm, chan, chan_near, stages):
    local_len, batch_dev, width_dev = contexts.shape
    own = jnp.stack([contexts, cotangent]).transpose(0, 2, 1, 3)
    pair = lax.all_gather(own, TM, axis=2, tiled=True)
    whole_x, whole_dy = pair[0], pair[1]
    length = whole_x.shape[1]
    pre_time = jnp.einsum("tl,blc->btc", time_weight, whole_x, preferred_element_type=jnp.float32)
    act_time, slope_time = gelu_pair(pre_time)
    mixed = (whole_x.astype(jnp.float32) + act_time).astype(jnp.bfloat16)
    rows = batch_dev * length
    mixed_rows = mixed.reshape(rows, width_dev)
    grad_rows = whole_dy.reshape(rows, width_dev)
    hidden_part = jnp.dot(mixed_rows, w_in, preferred_element_type=jnp.float32)
    hgrad_part = jnp.einsum("rc,hc->rh", grad_rows, w_out, preferred_element_type=jnp.float32)
    summed = scatter_a2a(jnp.stack([hidden_part, hgrad_part], 1), "cx", chan_near)
    summed = scatter_a2a(summed, "zh", chan // chan_near)
    act_rows, pre_grad_rows = hidden_finish(summed[:, 0], summed[:, 1])
    fin = gather_a2a(jnp.stack([act_rows, pre_grad_rows], 1), "zh", chan // chan_near)
    fin = gather_a2a(fin, "cx", chan_near)
    activation, pre_grad = fin[:, 0], fin[:, 1]
    win_part = jnp.einsum("rc,rh->ch", mixed_rows, pre_grad, preferred_element_type=jnp.float32)
    wout_part = jnp.einsum("rh,rc->hc", activation, grad_rows, preferred_element_type=jnp.float32)
    grad_w_in, grad_w_out = (
        lax.psum_scatter(win_part, "dp", scatter_dimension=1, tiled=True),
        lax.psum_scatter(wout_part, "dp", scatter_dimension=0, tiled=True),
    )
    share = jnp.einsum("rh,ch->rc", pre_grad, w_in, preferred_element_type=jnp.float32) + grad_rows.astype(
        jnp.float32
    ) * (1.0 / tm)
    share = share.reshape(batch_dev, length, width_dev)
    gate = (share * slope_time).astype(jnp.bfloat16)
    back = jnp.einsum("tl,btc->blc", time_weight, gate, preferred_element_type=jnp.float32)
    grad_own = lax.psum_scatter(share + back, TM, scatter_dimension=1, tiled=True)
    grad_contexts = grad_own.astype(jnp.bfloat16).transpose(1, 0, 2)
    time_part = jnp.einsum("btc,blc->tl", gate, whole_x, preferred_element_type=jnp.float32)
    for names, size in stages:
        time_part = scatter_a2a(time_part, names, size)
    for names, size in stages[::-1]:
        time_part = gather_a2a(time_part, names, size)
    grad_time = time_part
    return (grad_contexts, grad_w_in, grad_w_out, grad_time)


def solution(mesh):
    chan, tm, dp = mesh.shape["chan"], mesh.shape["tm"], mesh.shape["dp"]
    far, near_z = 2, 4
    fine = Mesh(
        mesh.devices.reshape(far, chan // far, near_z, tm // near_z, dp), ("zh", "cx", "tz", "ty", "dp")
    )
    step = functools.partial(
        on_device,
        tm=tm,
        chan=chan,
        chan_near=chan // far,
        stages=((("dp",), dp), (TM, tm), (CHAN, chan)),
    )
    token = P(TM, "dp", CHAN)
    return jax.shard_map(
        step,
        mesh=fine,
        in_specs=(token, token, P(CHAN, TM), P(TM, CHAN), P()),
        out_specs=(token, P(CHAN, TM + ("dp",)), P(TM + ("dp",), CHAN), P()),
        check_vma=False,
    )
```

```python
import functools
import math

import jax
import jax.numpy as jnp
from jax import lax
from jax.sharding import Mesh
from jax.sharding import PartitionSpec as P

TM = ("tz", "ty")
CHAN = ("zh", "cx")
tanh_scale = math.sqrt(2.0 / math.pi)
cubic_term = 0.044715


def gelu_pair(value):
    inner = jnp.tanh(tanh_scale * (value + cubic_term * value * value * value))
    result = 0.5 * value * (1.0 + inner)
    slope = 0.5 * (1.0 + inner) + 0.5 * value * (1.0 - inner * inner) * tanh_scale * (
        1.0 + 3.0 * cubic_term * value * value
    )
    return (result, slope)


def hidden_finish(hidden_pre, hidden_grad):
    act_hidden, slope_hidden = gelu_pair(hidden_pre)
    return (act_hidden.astype(jnp.bfloat16), (hidden_grad * slope_hidden).astype(jnp.bfloat16))


def gather_a2a(x, axis_name, size):
    b = jnp.broadcast_to(x[None], (size,) + x.shape)
    y = lax.all_to_all(b, axis_name, 0, 0, tiled=True)
    return y.reshape((size * x.shape[0],) + x.shape[1:])


def scatter_a2a(p, axis_name, size):
    y = lax.all_to_all(p.reshape((size, p.shape[0] // size) + p.shape[1:]), axis_name, 0, 0, tiled=True)
    return y.sum(0)


def on_device(contexts, cotangent, w_in, w_out, time_weight, tm, chan, chan_near, dp, stages):
    local_len, batch_dev, width_dev = contexts.shape
    own = jnp.stack([contexts, cotangent]).transpose(0, 2, 1, 3)
    pair = lax.all_gather(own, TM, axis=2, tiled=True)
    whole_x, whole_dy = pair[0], pair[1]
    length = whole_x.shape[1]
    pre_time = jnp.einsum("tl,blc->btc", time_weight, whole_x, preferred_element_type=jnp.float32)
    act_time, slope_time = gelu_pair(pre_time)
    mixed = (whole_x.astype(jnp.float32) + act_time).astype(jnp.bfloat16)
    rows = batch_dev * length
    mixed_rows = mixed.reshape(rows, width_dev)
    grad_rows = whole_dy.reshape(rows, width_dev)
    hidden_part = jnp.dot(mixed_rows, w_in, preferred_element_type=jnp.float32)
    hgrad_part = jnp.einsum("rc,hc->rh", grad_rows, w_out, preferred_element_type=jnp.float32)
    summed = scatter_a2a(jnp.stack([hidden_part, hgrad_part], 1), "cx", chan_near)
    summed = scatter_a2a(summed, "zh", chan // chan_near)
    act_rows, pre_grad_rows = hidden_finish(summed[:, 0], summed[:, 1])
    fin = gather_a2a(jnp.stack([act_rows, pre_grad_rows], 1), "zh", chan // chan_near)
    fin = gather_a2a(fin, "cx", chan_near)
    activation, pre_grad = fin[:, 0], fin[:, 1]
    hidden_dev = pre_grad.shape[1]
    win_part = jnp.einsum(
        "rc,rkh->kch",
        mixed_rows,
        pre_grad.reshape(rows, dp, hidden_dev // dp),
        preferred_element_type=jnp.float32,
    )
    wout_part = jnp.einsum("rh,rc->hc", activation, grad_rows, preferred_element_type=jnp.float32)
    grad_w_in = scatter_a2a(win_part.reshape(dp * width_dev, hidden_dev // dp), "dp", dp)
    grad_w_out = scatter_a2a(wout_part, "dp", dp)
    share = jnp.einsum("rh,ch->rc", pre_grad, w_in, preferred_element_type=jnp.float32) + grad_rows.astype(
        jnp.float32
    ) * (1.0 / tm)
    share = share.reshape(batch_dev, length, width_dev)
    gate = (share * slope_time).astype(jnp.bfloat16)
    back = jnp.einsum("tl,btc->blc", time_weight, gate, preferred_element_type=jnp.float32)
    grad_own = lax.psum_scatter(share + back, TM, scatter_dimension=1, tiled=True)
    grad_contexts = grad_own.astype(jnp.bfloat16).transpose(1, 0, 2)
    time_part = jnp.einsum("btc,blc->tl", gate, whole_x, preferred_element_type=jnp.float32)
    for names, size in stages:
        time_part = scatter_a2a(time_part, names, size)
    for names, size in stages[::-1]:
        time_part = gather_a2a(time_part, names, size)
    grad_time = time_part
    return (grad_contexts, grad_w_in, grad_w_out, grad_time)


def solution(mesh):
    chan, tm, dp = mesh.shape["chan"], mesh.shape["tm"], mesh.shape["dp"]
    far, near_z = 2, 4
    fine = Mesh(
        mesh.devices.reshape(far, chan // far, near_z, tm // near_z, dp), ("zh", "cx", "tz", "ty", "dp")
    )
    step = functools.partial(
        on_device,
        tm=tm,
        chan=chan,
        chan_near=chan // far,
        dp=dp,
        stages=(("dp", dp), ("cx", chan // far), ("zh", far), (TM, tm)),
    )
    token = P(TM, "dp", CHAN)
    return jax.shard_map(
        step,
        mesh=fine,
        in_specs=(token, token, P(CHAN, TM), P(TM, CHAN), P()),
        out_specs=(token, P(CHAN, TM + ("dp",)), P(TM + ("dp",), CHAN), P()),
        check_vma=False,
    )
```

```python
import functools
import math

import jax
import jax.numpy as jnp
from jax import lax
from jax.sharding import Mesh
from jax.sharding import PartitionSpec as P

TM = ("tz", "ty")
TM_SIZES = (4, 4)
CHAN = ("zh", "cx")
tanh_scale = math.sqrt(2.0 / math.pi)
cubic_term = 0.044715


def gelu_pair(value):
    inner = jnp.tanh(tanh_scale * (value + cubic_term * value * value * value))
    result = 0.5 * value * (1.0 + inner)
    slope = 0.5 * (1.0 + inner) + 0.5 * value * (1.0 - inner * inner) * tanh_scale * (
        1.0 + 3.0 * cubic_term * value * value
    )
    return (result, slope)


def hidden_finish(hidden_pre, hidden_grad):
    act_hidden, slope_hidden = gelu_pair(hidden_pre)
    return (act_hidden.astype(jnp.bfloat16), (hidden_grad * slope_hidden).astype(jnp.bfloat16))


def gather_a2a(x, axis_name, size):
    b = jnp.broadcast_to(x[None], (size,) + x.shape)
    y = lax.all_to_all(b, axis_name, 0, 0, tiled=True)
    return y.reshape((size * x.shape[0],) + x.shape[1:])


def scatter_a2a(p, axis_name, size):
    y = lax.all_to_all(p.reshape((size, p.shape[0] // size) + p.shape[1:]), axis_name, 0, 0, tiled=True)
    return y.sum(0)


def on_device(contexts, cotangent, w_in, w_out, time_weight, tm, chan, chan_near, stages):
    local_len, batch_dev, width_dev = contexts.shape
    own = jnp.stack([contexts, cotangent]).transpose(0, 2, 1, 3)
    pair = lax.all_gather(own, TM, axis=2, tiled=True)
    whole_x, whole_dy = pair[0], pair[1]
    length = whole_x.shape[1]
    pre_time = jnp.einsum("tl,blc->btc", time_weight, whole_x, preferred_element_type=jnp.float32)
    act_time, slope_time = gelu_pair(pre_time)
    mixed = (whole_x.astype(jnp.float32) + act_time).astype(jnp.bfloat16)
    rows = batch_dev * length
    mixed_rows = mixed.reshape(rows, width_dev)
    grad_rows = whole_dy.reshape(rows, width_dev)
    hidden_part = jnp.dot(mixed_rows, w_in, preferred_element_type=jnp.float32)
    hgrad_part = jnp.einsum("rc,hc->rh", grad_rows, w_out, preferred_element_type=jnp.float32)
    summed = scatter_a2a(jnp.stack([hidden_part, hgrad_part], 1), "cx", chan_near)
    summed = scatter_a2a(summed, "zh", chan // chan_near)
    act_rows, pre_grad_rows = hidden_finish(summed[:, 0], summed[:, 1])
    fin = gather_a2a(jnp.stack([act_rows, pre_grad_rows], 1), "zh", chan // chan_near)
    fin = gather_a2a(fin, "cx", chan_near)
    activation, pre_grad = fin[:, 0], fin[:, 1]
    win_part = jnp.einsum("rc,rh->ch", mixed_rows, pre_grad, preferred_element_type=jnp.float32)
    wout_part = jnp.einsum("rh,rc->hc", activation, grad_rows, preferred_element_type=jnp.float32)
    grad_w_in, grad_w_out = (
        lax.psum_scatter(win_part, "dp", scatter_dimension=1, tiled=True),
        lax.psum_scatter(wout_part, "dp", scatter_dimension=0, tiled=True),
    )
    share = jnp.einsum("rh,ch->rc", pre_grad, w_in, preferred_element_type=jnp.float32) + grad_rows.astype(
        jnp.float32
    ) * (1.0 / tm)
    share = share.reshape(batch_dev, length, width_dev)
    gate = (share * slope_time).astype(jnp.bfloat16)
    back = jnp.einsum("tl,btc->blc", time_weight, gate, preferred_element_type=jnp.float32)
    near_z = TM_SIZES[0]
    grad_own = (share + back).reshape(batch_dev, near_z, tm // near_z, local_len, width_dev)
    grad_own = lax.psum_scatter(grad_own, "ty", scatter_dimension=2, tiled=True)
    grad_own = lax.psum_scatter(grad_own, "tz", scatter_dimension=1, tiled=True)
    grad_contexts = grad_own.reshape(batch_dev, local_len, width_dev).astype(jnp.bfloat16).transpose(1, 0, 2)
    time_part = jnp.einsum("btc,blc->tl", gate, whole_x, preferred_element_type=jnp.float32)
    for names, size in stages:
        time_part = scatter_a2a(time_part, names, size)
    for names, size in stages[::-1]:
        time_part = gather_a2a(time_part, names, size)
    grad_time = time_part
    return (grad_contexts, grad_w_in, grad_w_out, grad_time)


def solution(mesh):
    chan, tm, dp = mesh.shape["chan"], mesh.shape["tm"], mesh.shape["dp"]
    far, near_z = 2, TM_SIZES[0]
    fine = Mesh(
        mesh.devices.reshape(far, chan // far, near_z, tm // near_z, dp), ("zh", "cx", "tz", "ty", "dp")
    )
    step = functools.partial(
        on_device,
        tm=tm,
        chan=chan,
        chan_near=chan // far,
        stages=((("dp",), dp), (TM, tm), (CHAN, chan)),
    )
    token = P(TM, "dp", CHAN)
    return jax.shard_map(
        step,
        mesh=fine,
        in_specs=(token, token, P(CHAN, TM), P(TM, CHAN), P()),
        out_specs=(token, P(CHAN, TM + ("dp",)), P(TM + ("dp",), CHAN), P()),
        check_vma=False,
    )
```

```python
import functools
import math

import jax
import jax.numpy as jnp
from jax import lax
from jax.sharding import Mesh
from jax.sharding import PartitionSpec as P

TM = ("tz", "ty")
CHAN = ("zh", "cx")
tanh_scale = math.sqrt(2.0 / math.pi)
cubic_term = 0.044715


def gelu_pair(value):
    inner = jnp.tanh(tanh_scale * (value + cubic_term * value * value * value))
    result = 0.5 * value * (1.0 + inner)
    slope = 0.5 * (1.0 + inner) + 0.5 * value * (1.0 - inner * inner) * tanh_scale * (
        1.0 + 3.0 * cubic_term * value * value
    )
    return (result, slope)


def hidden_finish(hidden_pre, hidden_grad):
    act_hidden, slope_hidden = gelu_pair(hidden_pre)
    return (act_hidden.astype(jnp.bfloat16), (hidden_grad * slope_hidden).astype(jnp.bfloat16))


def gather_a2a(x, axis_name, size):
    b = jnp.broadcast_to(x[None], (size,) + x.shape)
    y = lax.all_to_all(b, axis_name, 0, 0, tiled=True)
    return y.reshape((size * x.shape[0],) + x.shape[1:])


def scatter_a2a(p, axis_name, size):
    y = lax.all_to_all(p.reshape((size, p.shape[0] // size) + p.shape[1:]), axis_name, 0, 0, tiled=True)
    return y.sum(0)


def on_device(contexts, cotangent, w_in, w_out, time_weight, tm, chan, chan_near, stages):
    local_len, batch_dev, width_dev = contexts.shape
    own = jnp.stack([contexts, cotangent]).transpose(0, 2, 1, 3)
    pair = lax.all_gather(own, TM, axis=2, tiled=True)
    whole_x, whole_dy = pair[0], pair[1]
    length = whole_x.shape[1]
    pre_time = jnp.einsum("tl,blc->btc", time_weight, whole_x, preferred_element_type=jnp.float32)
    act_time, slope_time = gelu_pair(pre_time)
    mixed = (whole_x.astype(jnp.float32) + act_time).astype(jnp.bfloat16)
    rows = batch_dev * length
    mixed_rows = mixed.reshape(rows, width_dev)
    grad_rows = whole_dy.reshape(rows, width_dev)
    hidden_part = jnp.dot(mixed_rows, w_in, preferred_element_type=jnp.float32)
    hgrad_part = jnp.einsum("rc,hc->rh", grad_rows, w_out, preferred_element_type=jnp.float32)
    summed = scatter_a2a(jnp.stack([hidden_part, hgrad_part], 1), "cx", chan_near)
    summed = scatter_a2a(summed, "zh", chan // chan_near)
    act_rows, pre_grad_rows = hidden_finish(summed[:, 0], summed[:, 1])
    fin = gather_a2a(jnp.stack([act_rows, pre_grad_rows], 1), "zh", chan // chan_near)
    fin = gather_a2a(fin, "cx", chan_near)
    activation, pre_grad = fin[:, 0], fin[:, 1]
    win_part = jnp.einsum("rc,rh->ch", mixed_rows, pre_grad, preferred_element_type=jnp.float32)
    wout_part = jnp.einsum("rh,rc->hc", activation, grad_rows, preferred_element_type=jnp.float32)
    grad_w_in, grad_w_out = (
        lax.psum_scatter(win_part, "dp", scatter_dimension=1, tiled=True),
        lax.psum_scatter(wout_part, "dp", scatter_dimension=0, tiled=True),
    )
    share = jnp.einsum("rh,ch->rc", pre_grad, w_in, preferred_element_type=jnp.float32) + grad_rows.astype(
        jnp.float32
    ) * (1.0 / tm)
    share = share.reshape(batch_dev, length, width_dev)
    gate = (share * slope_time).astype(jnp.bfloat16)
    back = jnp.einsum("tl,btc->blc", time_weight, gate, preferred_element_type=jnp.float32)
    grad_own = lax.psum_scatter(share + back, TM, scatter_dimension=1, tiled=True)
    grad_contexts = grad_own.astype(jnp.bfloat16).transpose(1, 0, 2)
    time_part = jnp.einsum("btc,blc->tl", gate, whole_x, preferred_element_type=jnp.float32)
    for names, size in stages:
        time_part = scatter_a2a(time_part, names, size)
    for names, size in stages[::-1]:
        time_part = gather_a2a(time_part, names, size)
    grad_time = time_part
    return (grad_contexts, grad_w_in, grad_w_out, grad_time)


def solution(mesh):
    chan, tm, dp = mesh.shape["chan"], mesh.shape["tm"], mesh.shape["dp"]
    far, near_z = 2, 4
    fine = Mesh(
        mesh.devices.reshape(far, chan // far, near_z, tm // near_z, dp), ("zh", "cx", "tz", "ty", "dp")
    )
    step = functools.partial(
        on_device,
        tm=tm,
        chan=chan,
        chan_near=chan // far,
        stages=((CHAN + TM + ("dp",), mesh.size),),
    )
    token = P(TM, "dp", CHAN)
    return jax.shard_map(
        step,
        mesh=fine,
        in_specs=(token, token, P(CHAN, TM), P(TM, CHAN), P()),
        out_specs=(token, P(CHAN, TM + ("dp",)), P(TM + ("dp",), CHAN), P()),
        check_vma=False,
    )
```

```python
import functools
import math

import jax
import jax.numpy as jnp
from jax import lax
from jax.sharding import Mesh
from jax.sharding import PartitionSpec as P

TM = ("tz", "ty")
CHAN = ("zh", "cx")
tanh_scale = math.sqrt(2.0 / math.pi)
cubic_term = 0.044715


def gelu_pair(value):
    inner = jnp.tanh(tanh_scale * (value + cubic_term * value * value * value))
    result = 0.5 * value * (1.0 + inner)
    slope = 0.5 * (1.0 + inner) + 0.5 * value * (1.0 - inner * inner) * tanh_scale * (
        1.0 + 3.0 * cubic_term * value * value
    )
    return (result, slope)


def hidden_finish(hidden_pre, hidden_grad):
    act_hidden, slope_hidden = gelu_pair(hidden_pre)
    return (act_hidden.astype(jnp.bfloat16), (hidden_grad * slope_hidden).astype(jnp.bfloat16))


def gather_a2a(x, axis_name, size):
    b = jnp.broadcast_to(x[None], (size,) + x.shape)
    y = lax.all_to_all(b, axis_name, 0, 0, tiled=True)
    return y.reshape((size * x.shape[0],) + x.shape[1:])


def scatter_a2a(p, axis_name, size):
    y = lax.all_to_all(p.reshape((size, p.shape[0] // size) + p.shape[1:]), axis_name, 0, 0, tiled=True)
    return y.sum(0)


def on_device(contexts, cotangent, w_in, w_out, time_weight, tm, chan, chan_near, stages):
    local_len, batch_dev, width_dev = contexts.shape
    own = jnp.stack([contexts, cotangent]).transpose(0, 2, 1, 3)
    pair = lax.all_gather(own, TM, axis=2, tiled=True)
    whole_x, whole_dy = pair[0], pair[1]
    length = whole_x.shape[1]
    pre_time = jnp.einsum("tl,blc->btc", time_weight, whole_x, preferred_element_type=jnp.float32)
    act_time, slope_time = gelu_pair(pre_time)
    mixed = (whole_x.astype(jnp.float32) + act_time).astype(jnp.bfloat16)
    rows = batch_dev * length
    mixed_rows = mixed.reshape(rows, width_dev)
    grad_rows = whole_dy.reshape(rows, width_dev)
    hidden_part = jnp.dot(mixed_rows, w_in, preferred_element_type=jnp.float32)
    hgrad_part = jnp.einsum("rc,hc->rh", grad_rows, w_out, preferred_element_type=jnp.float32)
    hidden_pre = lax.psum_scatter(hidden_part, "cx", scatter_dimension=0, tiled=True)
    hidden_pre = lax.psum_scatter(hidden_pre, "zh", scatter_dimension=0, tiled=True)
    hidden_grad = scatter_a2a(hgrad_part, "cx", chan_near)
    hidden_grad = scatter_a2a(hidden_grad, "zh", chan // chan_near)
    act_rows, pre_grad_rows = hidden_finish(hidden_pre, hidden_grad)
    activation = lax.all_gather(act_rows, "zh", axis=0, tiled=True)
    activation = lax.all_gather(activation, "cx", axis=0, tiled=True)
    pre_grad = gather_a2a(pre_grad_rows, "zh", chan // chan_near)
    pre_grad = gather_a2a(pre_grad, "cx", chan_near)
    win_part = jnp.einsum("rc,rh->ch", mixed_rows, pre_grad, preferred_element_type=jnp.float32)
    wout_part = jnp.einsum("rh,rc->hc", activation, grad_rows, preferred_element_type=jnp.float32)
    grad_w_in, grad_w_out = (
        lax.psum_scatter(win_part, "dp", scatter_dimension=1, tiled=True),
        lax.psum_scatter(wout_part, "dp", scatter_dimension=0, tiled=True),
    )
    share = jnp.einsum("rh,ch->rc", pre_grad, w_in, preferred_element_type=jnp.float32) + grad_rows.astype(
        jnp.float32
    ) * (1.0 / tm)
    share = share.reshape(batch_dev, length, width_dev)
    gate = (share * slope_time).astype(jnp.bfloat16)
    back = jnp.einsum("tl,btc->blc", time_weight, gate, preferred_element_type=jnp.float32)
    grad_own = lax.psum_scatter(share + back, TM, scatter_dimension=1, tiled=True)
    grad_contexts = grad_own.astype(jnp.bfloat16).transpose(1, 0, 2)
    time_part = jnp.einsum("btc,blc->tl", gate, whole_x, preferred_element_type=jnp.float32)
    for names, size in stages:
        time_part = scatter_a2a(time_part, names, size)
    for names, size in stages[::-1]:
        time_part = gather_a2a(time_part, names, size)
    grad_time = time_part
    return (grad_contexts, grad_w_in, grad_w_out, grad_time)


def solution(mesh):
    chan, tm, dp = mesh.shape["chan"], mesh.shape["tm"], mesh.shape["dp"]
    far, near_z = 2, 4
    fine = Mesh(
        mesh.devices.reshape(far, chan // far, near_z, tm // near_z, dp), ("zh", "cx", "tz", "ty", "dp")
    )
    step = functools.partial(
        on_device,
        tm=tm,
        chan=chan,
        chan_near=chan // far,
        stages=((("dp",), dp), (TM, tm), (CHAN, chan)),
    )
    token = P(TM, "dp", CHAN)
    return jax.shard_map(
        step,
        mesh=fine,
        in_specs=(token, token, P(CHAN, TM), P(TM, CHAN), P()),
        out_specs=(token, P(CHAN, TM + ("dp",)), P(TM + ("dp",), CHAN), P()),
        check_vma=False,
    )
```

```python
import functools
import math

import jax
import jax.numpy as jnp
from jax import lax
from jax.sharding import Mesh
from jax.sharding import PartitionSpec as P

TM = ("tz", "ty")
CHAN = ("zh", "cx")
tanh_scale = math.sqrt(2.0 / math.pi)
cubic_term = 0.044715


def gelu_pair(value):
    inner = jnp.tanh(tanh_scale * (value + cubic_term * value * value * value))
    result = 0.5 * value * (1.0 + inner)
    slope = 0.5 * (1.0 + inner) + 0.5 * value * (1.0 - inner * inner) * tanh_scale * (
        1.0 + 3.0 * cubic_term * value * value
    )
    return (result, slope)


def hidden_finish(hidden_pre, hidden_grad):
    act_hidden, slope_hidden = gelu_pair(hidden_pre)
    return (act_hidden.astype(jnp.bfloat16), (hidden_grad * slope_hidden).astype(jnp.bfloat16))


def gather_a2a(x, axis_name, size):
    b = jnp.broadcast_to(x[None], (size,) + x.shape)
    y = lax.all_to_all(b, axis_name, 0, 0, tiled=True)
    return y.reshape((size * x.shape[0],) + x.shape[1:])


def scatter_a2a(p, axis_name, size):
    y = lax.all_to_all(p.reshape((size, p.shape[0] // size) + p.shape[1:]), axis_name, 0, 0, tiled=True)
    return y.sum(0)


def on_device(contexts, cotangent, w_in, w_out, time_weight, tm, chan, chan_near, stages):
    local_len, batch_dev, width_dev = contexts.shape
    own = jnp.stack([contexts, cotangent]).transpose(0, 2, 1, 3)
    pair = lax.all_gather(own, TM, axis=2, tiled=True)
    whole_x, whole_dy = pair[0], pair[1]
    length = whole_x.shape[1]
    pre_time = jnp.einsum("tl,blc->btc", time_weight, whole_x, preferred_element_type=jnp.float32)
    act_time, slope_time = gelu_pair(pre_time)
    mixed = (whole_x.astype(jnp.float32) + act_time).astype(jnp.bfloat16)
    rows = batch_dev * length
    mixed_rows = mixed.reshape(rows, width_dev)
    grad_rows = whole_dy.reshape(rows, width_dev)
    hidden_part = jnp.dot(mixed_rows, w_in, preferred_element_type=jnp.float32)
    hgrad_part = jnp.einsum("rc,hc->rh", grad_rows, w_out, preferred_element_type=jnp.float32)
    summed = scatter_a2a(jnp.stack([hidden_part, hgrad_part], 1), "cx", chan_near)
    summed = scatter_a2a(summed, "zh", chan // chan_near)
    act_rows, pre_grad_rows = hidden_finish(summed[:, 0], summed[:, 1])
    fin = gather_a2a(jnp.stack([act_rows, pre_grad_rows], 1), "zh", chan // chan_near)
    fin = gather_a2a(fin, "cx", chan_near)
    activation, pre_grad = fin[:, 0], fin[:, 1]
    win_part = jnp.einsum("rc,rh->ch", mixed_rows, pre_grad, preferred_element_type=jnp.float32)
    wout_part = jnp.einsum("rh,rc->hc", activation, grad_rows, preferred_element_type=jnp.float32)
    grad_w_in, grad_w_out = (
        lax.psum_scatter(win_part, "dp", scatter_dimension=1, tiled=True),
        lax.psum_scatter(wout_part, "dp", scatter_dimension=0, tiled=True),
    )
    share = jnp.einsum("rh,ch->rc", pre_grad, w_in, preferred_element_type=jnp.float32) + grad_rows.astype(
        jnp.float32
    ) * (1.0 / tm)
    share = share.reshape(batch_dev, length, width_dev)
    gate = (share * slope_time).astype(jnp.bfloat16)
    back = jnp.einsum("tl,btc->blc", time_weight, gate, preferred_element_type=jnp.float32)
    grad_own = lax.psum_scatter(share + back, TM, scatter_dimension=1, tiled=True)
    grad_contexts = grad_own.astype(jnp.bfloat16).transpose(1, 0, 2)
    time_part = jnp.einsum("btc,blc->tl", gate, whole_x, preferred_element_type=jnp.float32)
    for names, size in stages:
        time_part = scatter_a2a(time_part, names, size)
    for names, size in stages[::-1]:
        time_part = gather_a2a(time_part, names, size)
    grad_time = time_part
    return (grad_contexts, grad_w_in, grad_w_out, grad_time)


def solution(mesh):
    chan, tm, dp = mesh.shape["chan"], mesh.shape["tm"], mesh.shape["dp"]
    far, near_z = 2, 4
    fine = Mesh(
        mesh.devices.reshape(far, chan // far, near_z, tm // near_z, dp), ("zh", "cx", "tz", "ty", "dp")
    )
    step = functools.partial(
        on_device,
        tm=tm,
        chan=chan,
        chan_near=chan // far,
        stages=((("dp",), dp), (("cx",), chan // far), (("zh",), far), (TM, tm)),
    )
    token = P(TM, "dp", CHAN)
    return jax.shard_map(
        step,
        mesh=fine,
        in_specs=(token, token, P(CHAN, TM), P(TM, CHAN), P()),
        out_specs=(token, P(CHAN, TM + ("dp",)), P(TM + ("dp",), CHAN), P()),
        check_vma=False,
    )
```

```python
import functools
import math

import jax
import jax.numpy as jnp
from jax import lax
from jax.sharding import Mesh
from jax.sharding import PartitionSpec as P

TM = ("tz", "ty")
CHAN = ("zh", "cx")
tanh_scale = math.sqrt(2.0 / math.pi)
cubic_term = 0.044715


def gelu_pair(value):
    inner = jnp.tanh(tanh_scale * (value + cubic_term * value * value * value))
    result = 0.5 * value * (1.0 + inner)
    slope = 0.5 * (1.0 + inner) + 0.5 * value * (1.0 - inner * inner) * tanh_scale * (
        1.0 + 3.0 * cubic_term * value * value
    )
    return (result, slope)


def hidden_finish(hidden_pre, hidden_grad):
    act_hidden, slope_hidden = gelu_pair(hidden_pre)
    return (act_hidden.astype(jnp.bfloat16), (hidden_grad * slope_hidden).astype(jnp.bfloat16))


def gather_a2a(x, axis_name, size):
    b = jnp.broadcast_to(x[None], (size,) + x.shape)
    y = lax.all_to_all(b, axis_name, 0, 0, tiled=True)
    return y.reshape((size * x.shape[0],) + x.shape[1:])


def scatter_a2a(p, axis_name, size):
    y = lax.all_to_all(p.reshape((size, p.shape[0] // size) + p.shape[1:]), axis_name, 0, 0, tiled=True)
    return y.sum(0)


def on_device(contexts, cotangent, w_in, w_out, time_weight, tm, chan, chan_near, stages):
    local_len, batch_dev, width_dev = contexts.shape
    own = jnp.stack([contexts, cotangent]).transpose(0, 2, 1, 3)
    pair = lax.all_gather(own, TM, axis=2, tiled=True)
    whole_x, whole_dy = pair[0], pair[1]
    length = whole_x.shape[1]
    pre_time = jnp.einsum("tl,blc->btc", time_weight, whole_x, preferred_element_type=jnp.float32)
    act_time, slope_time = gelu_pair(pre_time)
    mixed = (whole_x.astype(jnp.float32) + act_time).astype(jnp.bfloat16)
    rows = batch_dev * length
    mixed_rows = mixed.reshape(rows, width_dev)
    grad_rows = whole_dy.reshape(rows, width_dev)
    hidden_part = jnp.dot(mixed_rows, w_in, preferred_element_type=jnp.float32)
    hgrad_part = jnp.einsum("rc,hc->rh", grad_rows, w_out, preferred_element_type=jnp.float32)
    summed = scatter_a2a(jnp.stack([hidden_part, hgrad_part], 1), "cx", chan_near)
    summed = scatter_a2a(summed, "zh", chan // chan_near)
    act_rows, pre_grad_rows = hidden_finish(summed[:, 0], summed[:, 1])
    fin = gather_a2a(jnp.stack([act_rows, pre_grad_rows], 1), "zh", chan // chan_near)
    fin = gather_a2a(fin, "cx", chan_near)
    activation, pre_grad = fin[:, 0], fin[:, 1]
    win_part = jnp.einsum("rc,rh->ch", mixed_rows, pre_grad, preferred_element_type=jnp.float32)
    wout_part = jnp.einsum("rh,rc->hc", activation, grad_rows, preferred_element_type=jnp.float32)
    grad_w_in, grad_w_out = (
        lax.psum_scatter(win_part, "dp", scatter_dimension=1, tiled=True),
        scatter_a2a(wout_part, "dp", 2),
    )
    share = jnp.einsum("rh,ch->rc", pre_grad, w_in, preferred_element_type=jnp.float32) + grad_rows.astype(
        jnp.float32
    ) * (1.0 / tm)
    share = share.reshape(batch_dev, length, width_dev)
    gate = (share * slope_time).astype(jnp.bfloat16)
    back = jnp.einsum("tl,btc->blc", time_weight, gate, preferred_element_type=jnp.float32)
    grad_own = lax.psum_scatter(share + back, TM, scatter_dimension=1, tiled=True)
    grad_contexts = grad_own.astype(jnp.bfloat16).transpose(1, 0, 2)
    time_part = jnp.einsum("btc,blc->tl", gate, whole_x, preferred_element_type=jnp.float32)
    for names, size in stages:
        time_part = scatter_a2a(time_part, names, size)
    for names, size in stages[::-1]:
        time_part = gather_a2a(time_part, names, size)
    grad_time = time_part
    return (grad_contexts, grad_w_in, grad_w_out, grad_time)


def solution(mesh):
    chan, tm, dp = mesh.shape["chan"], mesh.shape["tm"], mesh.shape["dp"]
    far, near_z = 2, 4
    fine = Mesh(
        mesh.devices.reshape(far, chan // far, near_z, tm // near_z, dp), ("zh", "cx", "tz", "ty", "dp")
    )
    step = functools.partial(
        on_device,
        tm=tm,
        chan=chan,
        chan_near=chan // far,
        stages=(
            (("dp",), dp),
            (("cx",), chan // far),
            (("zh",), far),
            (("ty",), tm // near_z),
            (("tz",), near_z),
        ),
    )
    token = P(TM, "dp", CHAN)
    return jax.shard_map(
        step,
        mesh=fine,
        in_specs=(token, token, P(CHAN, TM), P(TM, CHAN), P()),
        out_specs=(token, P(CHAN, TM + ("dp",)), P(TM + ("dp",), CHAN), P()),
        check_vma=False,
    )
```
